32 devices in a mesh: row: 4 (over y, x), col: 8 (over z, core).
Axes of the slice: x: 2, y: 2, z: 4, core: 2. Of those that a mesh axis runs over, the one named last changes fastest.
Arguments:
- sensitivity: bfloat16 [8192, 8, 4096], P('row', None, 'col'), may hold values from -0.25 to 0.25
- sample_weight: float32 [8192], P('row'), may hold values from 0.2 to 5
- pattern: int32 [16, 8, 8], P('row', None, 'col'), may hold values 0 or 1
- prior: float32 [2048], P('row'), may hold values from 0.5 to 5
Outputs:
- factored_band: float32 [2048, 8, 4096], P('row', None, 'col')
The draws below stay inside these ranges and needn't reach their ends.
Inputs may be any that keep to these rules, and one draw needn't show every extreme that they name: pattern holds only 0 and 1.
All inputs are finite; a program needn't handle non-finite values. No bound on the sum of `pattern` on one device may be relied on, other than what follows from the above.
Results may differ from the reference program's by a relative error of at most 0.0028.
Values may be sent and summed in bfloat16 or wider, within the bound.
No kernel may reach another device: no remote copies, remote signals or barrier semaphores. Data moves between devices by JAX's collectives and lax.ppermute only.
A program may use at most 128 MiB of HBM per device.

```python
import math
import jax
import jax.numpy as jnp
from jax import lax

TILE = 512
P_SIZE = 32768
SAMPLES = 8192
SBLK = 16
BAND = 2048
CYCLES = 8
N_COL = 8


def set_ends(result, own_key, least, high):
    longest = result.shape.index(max(result.shape))
    spots = []
    for shift in (0, 1):
        where = [jax.random.randint(jax.random.fold_in(own_key, axis), (), 0, length) for axis, length in enumerate(result.shape)]
        where[longest] = (where[longest] + shift) % result.shape[longest]
        spots.append(tuple(where))
    return result.at[spots[0]].set(least).at[spots[1]].set(high)


def steps_of(stream_key, shape, pieces, smallest, largest):
    loudness = 1.0
    for axis_at, parts in pieces:
        draws = jax.random.uniform(jax.random.fold_in(jax.random.fold_in(stream_key, 6), axis_at), (parts,), jnp.float32, smallest / len(pieces), largest / len(pieces))
        loudness = loudness * jnp.repeat(jnp.exp(draws), shape[axis_at] // parts).reshape((-1,) + (1,) * (len(shape) - 1 - axis_at))
    return loudness


def scatter_about(own_key, dims, scale, limit, shards=(), held_as=jnp.bfloat16):
    entries = scale * jax.random.normal(own_key, dims, jnp.float32)
    if shards:
        entries = entries * steps_of(own_key, dims, shards, -0.22, 0.18)
    return jnp.clip(entries, -limit, limit).astype(held_as)


def setup_inputs(seed: int = 0) -> dict:
    arg_keys = jax.random.split(jax.random.key(seed), 5)
    return {
        "sensitivity": scatter_about(arg_keys[0], (SAMPLES, CYCLES, N_COL * TILE), TILE ** -0.5, 0.25, ((0, 4), (2, 8))),
        "sample_weight": jnp.clip(jnp.exp(math.log(5.0) - 3.218876 * jax.random.uniform(arg_keys[1], (SAMPLES,), jnp.float32) ** steps_of(arg_keys[1], (SAMPLES,), ((0, 4),), -0.2, 0.2)), 0.2, 5.0),
        "pattern": set_ends((jax.random.randint(arg_keys[2], (SBLK, CYCLES, N_COL), 0, 2) < 1).astype(jnp.int32), jax.random.fold_in(arg_keys[2], 1), 0, 1),
        "prior": jnp.clip(jnp.exp(math.log(5.0) - 2.3025851 * jax.random.uniform(arg_keys[3], (BAND,), jnp.float32) ** steps_of(arg_keys[3], (BAND,), ((0, 4),), -0.2, 0.2)), 0.5, 5.0),
    }


def reference(sensitivity, sample_weight, pattern, prior):
    blocks = pattern.reshape(SAMPLES // TILE, P_SIZE // TILE).astype(jnp.bfloat16)
    masked = (sensitivity.reshape(SAMPLES // TILE, TILE, P_SIZE // TILE, TILE) * blocks[:, None, :, None]).reshape(SAMPLES, P_SIZE)
    weighted = (sample_weight[:, None] * masked.astype(jnp.float32)).astype(jnp.bfloat16)
    fisher = jnp.dot(masked[:, :BAND].T.astype(jnp.float32), weighted.astype(jnp.float32), preferred_element_type=jnp.float32)
    fisher = fisher.at[:, :BAND].add(jnp.diag(prior))
    lower = jnp.linalg.cholesky(fisher[:TILE, :TILE])
    panel = jax.scipy.linalg.solve_triangular(lower, fisher[:TILE], lower=True)
    updated = fisher[TILE:] - jnp.dot(panel[:, TILE:BAND].T, panel, precision=lax.Precision.HIGHEST)
    return jnp.concatenate([panel, updated], axis=0).reshape(BAND, CYCLES, -1)
```

```python
import jax
import jax.numpy as jnp
from jax import lax
from jax.sharding import PartitionSpec as P


def spread(value, axis, root):
    mine = lax.axis_index(axis) == root
    return lax.psum(jnp.where(mine, value, jnp.zeros_like(value)), axis)


def body(sensitivity, sample_weight, pattern, prior):
    rows_here = sensitivity.shape[0]
    cycles = sensitivity.shape[1]
    tile = sensitivity.shape[2]
    blocks = pattern.shape[0]
    widths = cycles * tile
    mask_blocks = pattern.astype(jnp.bfloat16)[:, None, :, :]
    masked = (sensitivity.reshape(blocks, tile, cycles, tile) * mask_blocks).reshape(
        rows_here, widths
    )
    weighted = (sample_weight[:, None] * masked.astype(jnp.float32)).astype(jnp.bfloat16)
    first_tile = masked[:, :tile]
    row_count = lax.axis_size("row")
    band_parts = []
    for owner in range(row_count):
        band_parts.append(spread(first_tile, "col", owner))
    band = jnp.concatenate(band_parts, axis=1)
    band_weighted = (sample_weight[:, None] * band.astype(jnp.float32)).astype(jnp.bfloat16)

    head = lax.psum(
        jnp.einsum("sb,sc->bc", band[:, :tile], band_weighted, preferred_element_type=jnp.float32),
        "row",
    )
    prior_head = lax.all_gather(prior, "row", tiled=True)[:tile]
    identity = jnp.eye(tile, dtype=jnp.float32)
    corner = head[:, :tile] + identity * prior_head[None, :]
    lower = jnp.linalg.cholesky(corner)
    lower_inv = jax.scipy.linalg.solve_triangular(lower, identity, lower=True)
    hi = lax.Precision.HIGHEST
    side_panel = jnp.dot(lower_inv, head[:, tile:], precision=hi)
    side_t = jnp.dot(side_panel.T, lower_inv, precision=hi)
    transform = jnp.concatenate([lower_inv, -side_t], axis=0)

    part_head = jnp.einsum(
        "sb,sc->bc", band[:, :tile], weighted, preferred_element_type=jnp.float32
    )
    part_rest = jnp.einsum(
        "sb,sc->bc", band[:, tile:], weighted, preferred_element_type=jnp.float32
    )
    moved = jnp.dot(transform, part_head, precision=lax.Precision.HIGH)
    partial = moved + jnp.concatenate(
        [jnp.zeros((tile, widths), jnp.float32), part_rest], axis=0
    )
    result = lax.psum_scatter(partial, "row", scatter_dimension=0, tiled=True)

    row = lax.axis_index("row")
    col = lax.axis_index("col")
    mine = lax.dynamic_slice_in_dim(transform, row * tile, tile, axis=0)
    head_on = (col == 0).astype(jnp.float32)
    diag_on = ((col == row) & (row != 0)).astype(jnp.float32)
    fix = head_on * mine * prior_head[None, :] + diag_on * identity * prior[None, :]
    result = result.at[:, :tile].add(fix)
    return result.reshape(tile, cycles, tile)


def solution(mesh):
    return jax.shard_map(
        body,
        mesh=mesh,
        in_specs=(P("row", None, "col"), P("row"), P("row", None, "col"), P("row")),
        out_specs=P("row", None, "col"),
        check_vma=False,
    )
```

```python
import jax
import jax.numpy as jnp
from jax import lax
from jax.sharding import PartitionSpec as P


def spread(value, axis, root):
    mine = lax.axis_index(axis) == root
    return lax.psum(jnp.where(mine, value, jnp.zeros_like(value)), axis)


def body(sensitivity, sample_weight, pattern, prior):
    rows_here = sensitivity.shape[0]
    cycles = sensitivity.shape[1]
    tile = sensitivity.shape[2]
    blocks = pattern.shape[0]
    widths = cycles * tile
    mask_blocks = pattern.astype(jnp.bfloat16)[:, None, :, :]
    masked = (sensitivity.reshape(blocks, tile, cycles, tile) * mask_blocks).reshape(
        rows_here, widths
    )
    weighted = (sample_weight[:, None] * masked.astype(jnp.float32)).astype(jnp.bfloat16)
    first_tile = masked[:, :tile]
    row_count = lax.axis_size("row")
    row = lax.axis_index("row")
    col = lax.axis_index("col")
    f32 = jnp.float32

    head_tile = spread(first_tile, "col", 0)
    block = jnp.einsum("sb,sc->bc", head_tile, weighted[:, :tile], preferred_element_type=f32)
    prior_row = jnp.where((row == 0) & (col == 0), prior, jnp.zeros_like(prior))
    extra = jnp.zeros((8, tile), f32).at[0].set(prior_row)
    ext = jnp.concatenate([block, extra], axis=0)
    slots = jnp.arange(row_count)[:, None, None]
    placed = jnp.where(slots == col, ext[None], jnp.zeros_like(ext)[None])
    head = lax.psum(placed, ("row", "col"))
    prior_head = head[0, tile]

    identity = jnp.eye(tile, dtype=f32)
    corner = head[0, :tile] + identity * prior_head[None, :]
    lower = jnp.linalg.cholesky(corner)
    lower_inv = jax.scipy.linalg.solve_triangular(lower, identity, lower=True)
    hi = lax.Precision.HIGHEST
    side_panel = jnp.einsum("ij,rjk->rik", lower_inv, head[1:, :tile], precision=hi)
    side_t = jnp.einsum("rji,jk->rik", side_panel, lower_inv, precision=hi)
    transform = jnp.concatenate(
        [lower_inv, -side_t.reshape((row_count - 1) * tile, tile)], axis=0
    )

    tile_src, head = lax.optimization_barrier((first_tile, head))
    rest_parts = [spread(tile_src, "col", owner) for owner in range(1, row_count)]
    rest = jnp.concatenate(rest_parts, axis=1)

    part_head = jnp.einsum("sb,sc->bc", head_tile, weighted, preferred_element_type=f32)
    part_rest = jnp.einsum("sb,sc->bc", rest, weighted, preferred_element_type=f32)
    chunks = 2 if cycles % 2 == 0 else 1
    span = widths // chunks
    pieces = []
    for k in range(chunks):
        cols_k = slice(k * span, (k + 1) * span)
        moved = jnp.dot(transform, part_head[:, cols_k], precision=lax.Precision.HIGH)
        partial = moved + jnp.concatenate(
            [jnp.zeros((tile, span), f32), part_rest[:, cols_k]], axis=0
        )
        pieces.append(lax.psum_scatter(partial, "row", scatter_dimension=0, tiled=True))
    result = jnp.concatenate(pieces, axis=1) if chunks > 1 else pieces[0]

    mine = lax.dynamic_slice_in_dim(transform, row * tile, tile, axis=0)
    head_on = (col == 0).astype(f32)
    diag_on = ((col == row) & (row != 0)).astype(f32)
    fix = head_on * mine * prior_head[None, :] + diag_on * identity * prior[None, :]
    result = result.at[:, :tile].add(fix)
    return result.reshape(tile, cycles, tile)


def solution(mesh):
    return jax.shard_map(
        body,
        mesh=mesh,
        in_specs=(P("row", None, "col"), P("row"), P("row", None, "col"), P("row")),
        out_specs=P("row", None, "col"),
        check_vma=False,
    )
```

```python
import jax
import jax.numpy as jnp
from jax import lax
from jax.sharding import PartitionSpec as P


def spread(value, axis, root):
    mine = lax.axis_index(axis) == root
    return lax.psum(jnp.where(mine, value, jnp.zeros_like(value)), axis)


def body(sensitivity, sample_weight, pattern, prior):
    rows_here = sensitivity.shape[0]
    cycles = sensitivity.shape[1]
    tile = sensitivity.shape[2]
    blocks = pattern.shape[0]
    widths = cycles * tile
    mask_blocks = pattern.astype(jnp.bfloat16)[:, None, :, :]
    masked = (sensitivity.reshape(blocks, tile, cycles, tile) * mask_blocks).reshape(
        rows_here, widths
    )
    weighted = (sample_weight[:, None] * masked.astype(jnp.float32)).astype(jnp.bfloat16)
    first_tile = masked[:, :tile]
    row_count = lax.axis_size("row")
    row = lax.axis_index("row")
    col = lax.axis_index("col")
    f32 = jnp.float32

    head_tile = spread(first_tile, "col", 0)
    head_weighted = (sample_weight[:, None] * head_tile.astype(f32)).astype(jnp.bfloat16)
    block = jnp.einsum("sb,sc->bc", head_tile, head_weighted, preferred_element_type=f32)
    prior_row = jnp.where(row == 0, prior, jnp.zeros_like(prior))
    extra = jnp.zeros((8, tile), f32).at[0].set(prior_row)
    corner_sum = lax.psum(jnp.concatenate([block, extra], axis=0), "row")
    prior_head = corner_sum[tile]

    identity = jnp.eye(tile, dtype=f32)
    corner = corner_sum[:tile] + identity * prior_head[None, :]
    lower = jnp.linalg.cholesky(corner)
    lower_inv = jax.scipy.linalg.solve_triangular(lower, identity, lower=True)

    tile_src, corner_sum = lax.optimization_barrier((first_tile, corner_sum))
    rest_parts = [spread(tile_src, "col", owner) for owner in range(1, row_count)]
    rest = jnp.concatenate(rest_parts, axis=1)
    rest_weighted = (sample_weight[:, None] * rest.astype(f32)).astype(jnp.bfloat16)
    side = lax.psum(
        jnp.einsum("sb,sc->bc", head_tile, rest_weighted, preferred_element_type=f32), "row"
    ).reshape(tile, row_count - 1, tile)

    hi = lax.Precision.HIGHEST
    side_panel = jnp.einsum("ij,jrk->rik", lower_inv, side, precision=hi)
    side_t = jnp.einsum("rji,jk->rik", side_panel, lower_inv, precision=hi)
    transform = jnp.concatenate(
        [lower_inv, -side_t.reshape((row_count - 1) * tile, tile)], axis=0
    )

    part_head = jnp.einsum("sb,sc->bc", head_tile, weighted, preferred_element_type=f32)
    part_rest = jnp.einsum("sb,sc->bc", rest, weighted, preferred_element_type=f32)
    chunks = 2 if cycles % 2 == 0 else 1
    span = widths // chunks
    pieces = []
    for k in range(chunks):
        cols_k = slice(k * span, (k + 1) * span)
        moved = jnp.dot(transform, part_head[:, cols_k], precision=lax.Precision.HIGH)
        partial = moved + jnp.concatenate(
            [jnp.zeros((tile, span), f32), part_rest[:, cols_k]], axis=0
        )
        pieces.append(lax.psum_scatter(partial, "row", scatter_dimension=0, tiled=True))
    result = jnp.concatenate(pieces, axis=1) if chunks > 1 else pieces[0]

    mine = lax.dynamic_slice_in_dim(transform, row * tile, tile, axis=0)
    head_on = (col == 0).astype(f32)
    diag_on = ((col == row) & (row != 0)).astype(f32)
    fix = head_on * mine * prior_head[None, :] + diag_on * identity * prior[None, :]
    result = result.at[:, :tile].add(fix)
    return result.reshape(tile, cycles, tile)


def solution(mesh):
    return jax.shard_map(
        body,
        mesh=mesh,
        in_specs=(P("row", None, "col"), P("row"), P("row", None, "col"), P("row")),
        out_specs=P("row", None, "col"),
        check_vma=False,
    )
```

```python
import jax
import jax.numpy as jnp
from jax import lax
from jax.sharding import PartitionSpec as P


def spread(value, axis, root):
    mine = lax.axis_index(axis) == root
    return lax.psum(jnp.where(mine, value, jnp.zeros_like(value)), axis)


def body(sensitivity, sample_weight, pattern, prior):
    rows_here = sensitivity.shape[0]
    cycles = sensitivity.shape[1]
    tile = sensitivity.shape[2]
    blocks = pattern.shape[0]
    widths = cycles * tile
    mask_blocks = pattern.astype(jnp.bfloat16)[:, None, :, :]
    masked = (sensitivity.reshape(blocks, tile, cycles, tile) * mask_blocks).reshape(
        rows_here, widths
    )
    weighted = (sample_weight[:, None] * masked.astype(jnp.float32)).astype(jnp.bfloat16)
    first_tile = (
        sensitivity[:, 0, :].reshape(blocks, tile, tile)
        * pattern[:, 0, :].astype(jnp.bfloat16)[:, :, None]
    ).reshape(rows_here, tile)
    row_count = lax.axis_size("row")
    row = lax.axis_index("row")
    col = lax.axis_index("col")
    f32 = jnp.float32

    head_tile = spread(first_tile, "col", 0)
    head_weighted = (sample_weight[:, None] * head_tile.astype(f32)).astype(jnp.bfloat16)
    block = jnp.einsum("sb,sc->bc", head_tile, head_weighted, preferred_element_type=f32)
    prior_row = jnp.where(row == 0, prior, jnp.zeros_like(prior))
    extra = jnp.zeros((8, tile), f32).at[0].set(prior_row)
    corner_sum = lax.psum(jnp.concatenate([block, extra], axis=0), "row")
    prior_head = corner_sum[tile]


    part_head = jnp.einsum("sb,sc->bc", head_tile, weighted, preferred_element_type=f32)

    tile_src, corner_sum, part_head = lax.optimization_barrier((first_tile, corner_sum, part_head))
    identity = jnp.eye(tile, dtype=f32)
    corner = corner_sum[:tile] + identity * prior_head[None, :]
    lower = jnp.linalg.cholesky(corner)
    lower_inv = jax.scipy.linalg.solve_triangular(lower, identity, lower=True)
    rest_parts = [spread(tile_src, "col", owner) for owner in range(1, row_count)]
    rest = jnp.concatenate(rest_parts, axis=1)
    rest, lower_inv = lax.optimization_barrier((rest, lower_inv))
    rest_weighted = (sample_weight[:, None] * rest.astype(f32)).astype(jnp.bfloat16)
    side = lax.psum(
        jnp.einsum("sb,sc->bc", head_tile, rest_weighted, preferred_element_type=f32), "row"
    ).reshape(tile, row_count - 1, tile)

    hi = lax.Precision.HIGHEST
    side_panel = jnp.einsum("ij,jrk->rik", lower_inv, side, precision=hi)
    side_t = jnp.einsum("rji,jk->rik", side_panel, lower_inv, precision=hi)
    transform = jnp.concatenate(
        [lower_inv, -side_t.reshape((row_count - 1) * tile, tile)], axis=0
    )

    part_rest = jnp.einsum("sb,sc->bc", rest, weighted, preferred_element_type=f32)
    chunks = 2 if cycles % 2 == 0 else 1
    span = widths // chunks
    pieces = []
    for k in range(chunks):
        cols_k = slice(k * span, (k + 1) * span)
        moved = jnp.dot(transform, part_head[:, cols_k], precision=lax.Precision.HIGH)
        partial = moved + jnp.concatenate(
            [jnp.zeros((tile, span), f32), part_rest[:, cols_k]], axis=0
        )
        pieces.append(lax.psum_scatter(partial, "row", scatter_dimension=0, tiled=True))
    result = jnp.concatenate(pieces, axis=1) if chunks > 1 else pieces[0]

    mine = lax.dynamic_slice_in_dim(transform, row * tile, tile, axis=0)
    head_on = (col == 0).astype(f32)
    diag_on = ((col == row) & (row != 0)).astype(f32)
    fix = head_on * mine * prior_head[None, :] + diag_on * identity * prior[None, :]
    result = result.at[:, :tile].add(fix)
    return result.reshape(tile, cycles, tile)


def solution(mesh):
    return jax.shard_map(
        body,
        mesh=mesh,
        in_specs=(P("row", None, "col"), P("row"), P("row", None, "col"), P("row")),
        out_specs=P("row", None, "col"),
        check_vma=False,
    )
```

```python
import jax
import jax.numpy as jnp
from jax import lax
from jax.sharding import PartitionSpec as P


def spread(value, axis, root):
    mine = lax.axis_index(axis) == root
    return lax.psum(jnp.where(mine, value, jnp.zeros_like(value)), axis)


def body(sensitivity, sample_weight, pattern, prior):
    rows_here = sensitivity.shape[0]
    cycles = sensitivity.shape[1]
    tile = sensitivity.shape[2]
    blocks = pattern.shape[0]
    widths = cycles * tile
    mask_blocks = pattern.astype(jnp.bfloat16)[:, None, :, :]
    masked = (sensitivity.reshape(blocks, tile, cycles, tile) * mask_blocks).reshape(
        rows_here, widths
    )
    weighted = (sample_weight[:, None] * masked.astype(jnp.float32)).astype(jnp.bfloat16)
    first_tile = (
        sensitivity[:, 0, :].reshape(blocks, tile, tile)
        * pattern[:, 0, :].astype(jnp.bfloat16)[:, :, None]
    ).reshape(rows_here, tile)
    row_count = lax.axis_size("row")
    row = lax.axis_index("row")
    col = lax.axis_index("col")
    f32 = jnp.float32

    head_tile = spread(first_tile, "col", 0)
    head_weighted = (sample_weight[:, None] * head_tile.astype(f32)).astype(jnp.bfloat16)
    block = jnp.einsum("sb,sc->bc", head_tile, head_weighted, preferred_element_type=f32)
    prior_row = jnp.where(row == 0, prior, jnp.zeros_like(prior))
    extra = jnp.zeros((8, tile), f32).at[0].set(prior_row)
    corner_sum = lax.psum(jnp.concatenate([block, extra], axis=0), "row")
    prior_head = corner_sum[tile]


    part_head = jnp.einsum("sb,sc->bc", head_tile, weighted, preferred_element_type=f32)

    tile_src, corner_sum, part_head = lax.optimization_barrier((first_tile, corner_sum, part_head))
    identity = jnp.eye(tile, dtype=f32)
    corner = corner_sum[:tile] + identity * prior_head[None, :]
    lower = jnp.linalg.cholesky(corner)
    lower_inv = jax.scipy.linalg.solve_triangular(lower, identity, lower=True)
    rest_parts = [spread(tile_src, "col", owner) for owner in range(1, row_count)]
    rest = jnp.concatenate(rest_parts, axis=1)
    rest, lower_inv = lax.optimization_barrier((rest, lower_inv))
    rest_weighted = (sample_weight[:, None] * rest.astype(f32)).astype(jnp.bfloat16)
    side = lax.psum(
        jnp.einsum("sb,sc->bc", head_tile, rest_weighted, preferred_element_type=f32), "row"
    ).reshape(tile, row_count - 1, tile)

    hi = lax.Precision.HIGHEST
    side_panel = jnp.einsum("ij,jrk->rik", lower_inv, side, precision=hi)
    side_t = jnp.einsum("rji,jk->rik", side_panel, lower_inv, precision=hi)
    transform = jnp.concatenate(
        [lower_inv, -side_t.reshape((row_count - 1) * tile, tile)], axis=0
    )

    part_rest = jnp.einsum("sb,sc->bc", rest, weighted, preferred_element_type=f32)
    chunks = 2 if cycles % 2 == 0 else 1
    span = widths // chunks
    mine = lax.dynamic_slice_in_dim(transform, row * tile, tile, axis=0)
    head_on = (col == 0).astype(f32)
    diag_on = ((col == row) & (row != 0)).astype(f32)
    fix = head_on * mine * prior_head[None, :] + diag_on * identity * prior[None, :]
    pieces = []
    for k in range(chunks):
        cols_k = slice(k * span, (k + 1) * span)
        moved = jnp.dot(transform, part_head[:, cols_k], precision=lax.Precision.HIGH)
        partial = moved + jnp.concatenate(
            [jnp.zeros((tile, span), f32), part_rest[:, cols_k]], axis=0
        )
        piece = lax.psum_scatter(partial, "row", scatter_dimension=0, tiled=True)
        if k == 0:
            piece = piece.at[:, :tile].add(fix)
        pieces.append(piece.reshape(tile, cycles // chunks, tile))
    return jnp.concatenate(pieces, axis=1) if chunks > 1 else pieces[0]


def solution(mesh):
    return jax.shard_map(
        body,
        mesh=mesh,
        in_specs=(P("row", None, "col"), P("row"), P("row", None, "col"), P("row")),
        out_specs=P("row", None, "col"),
        check_vma=False,
    )
```

```python
import jax
import jax.numpy as jnp
from jax import lax
from jax.sharding import PartitionSpec as P


def spread(value, axis, root):
    mine = lax.axis_index(axis) == root
    return lax.psum(jnp.where(mine, value, jnp.zeros_like(value)), axis)


def body(sensitivity, sample_weight, pattern, prior):
    rows_here = sensitivity.shape[0]
    cycles = sensitivity.shape[1]
    tile = sensitivity.shape[2]
    blocks = pattern.shape[0]
    widths = cycles * tile
    mask_blocks = pattern.astype(jnp.bfloat16)[:, None, :, :]
    masked = (sensitivity.reshape(blocks, tile, cycles, tile) * mask_blocks).reshape(
        rows_here, widths
    )
    weighted = (sample_weight[:, None] * masked.astype(jnp.float32)).astype(jnp.bfloat16)
    first_tile = (
        sensitivity[:, 0, :].reshape(blocks, tile, tile)
        * pattern[:, 0, :].astype(jnp.bfloat16)[:, :, None]
    ).reshape(rows_here, tile)
    row_count = lax.axis_size("row")
    row = lax.axis_index("row")
    col = lax.axis_index("col")
    f32 = jnp.float32

    head_tile = spread(first_tile, "col", 0)
    head_weighted = (sample_weight[:, None] * head_tile.astype(f32)).astype(jnp.bfloat16)
    block = jnp.einsum("sb,sc->bc", head_tile, head_weighted, preferred_element_type=f32)
    prior_row = jnp.where(row == 0, prior, jnp.zeros_like(prior))
    extra = jnp.zeros((8, tile), f32).at[0].set(prior_row)
    corner_sum = lax.psum(jnp.concatenate([block, extra], axis=0), "row")
    prior_head = corner_sum[tile]


    part_head = jnp.einsum("sb,sc->bc", head_tile, weighted, preferred_element_type=f32)

    tile_src, corner_sum, part_head = lax.optimization_barrier((first_tile, corner_sum, part_head))
    identity = jnp.eye(tile, dtype=f32)
    corner = corner_sum[:tile] + identity * prior_head[None, :]
    lower = jnp.linalg.cholesky(corner)
    lower_inv = jax.scipy.linalg.solve_triangular(lower, identity, lower=True)
    rest_parts = [spread(tile_src, "col", owner) for owner in range(1, row_count)]
    rest = jnp.concatenate(rest_parts, axis=1)
    rest, lower_inv = lax.optimization_barrier((rest, lower_inv))
    rest_weighted = (sample_weight[:, None] * rest.astype(f32)).astype(jnp.bfloat16)
    side = lax.psum(
        jnp.einsum("sb,sc->bc", head_tile, rest_weighted, preferred_element_type=f32), "row"
    ).reshape(tile, row_count - 1, tile)

    hi = lax.Precision.HIGHEST
    corner_inv = jnp.dot(lower_inv.T, lower_inv, precision=hi)
    side_t = jnp.einsum("jri,jk->rik", side, corner_inv, precision=hi)
    transform = jnp.concatenate(
        [lower_inv, -side_t.reshape((row_count - 1) * tile, tile)], axis=0
    )

    part_rest = jnp.einsum("sb,sc->bc", rest, weighted, preferred_element_type=f32)
    chunks = 2 if cycles % 2 == 0 else 1
    span = widths // chunks
    mine = lax.dynamic_slice_in_dim(transform, row * tile, tile, axis=0)
    head_on = (col == 0).astype(f32)
    diag_on = ((col == row) & (row != 0)).astype(f32)
    fix = head_on * mine * prior_head[None, :] + diag_on * identity * prior[None, :]
    pieces = []
    for k in range(chunks):
        cols_k = slice(k * span, (k + 1) * span)
        moved = jnp.dot(transform, part_head[:, cols_k], precision=lax.Precision.HIGH)
        partial = moved + jnp.concatenate(
            [jnp.zeros((tile, span), f32), part_rest[:, cols_k]], axis=0
        )
        piece = lax.psum_scatter(partial, "row", scatter_dimension=0, tiled=True)
        if k == 0:
            piece = piece.at[:, :tile].add(fix)
        pieces.append(piece.reshape(tile, cycles // chunks, tile))
    return jnp.concatenate(pieces, axis=1) if chunks > 1 else pieces[0]


def solution(mesh):
    return jax.shard_map(
        body,
        mesh=mesh,
        in_specs=(P("row", None, "col"), P("row"), P("row", None, "col"), P("row")),
        out_specs=P("row", None, "col"),
        check_vma=False,
    )
```

```python
import jax
import jax.numpy as jnp
from jax import lax
from jax.sharding import PartitionSpec as P


def spread(value, axis, root):
    mine = lax.axis_index(axis) == root
    return lax.psum(jnp.where(mine, value, jnp.zeros_like(value)), axis)


def body(sensitivity, sample_weight, pattern, prior):
    rows_here = sensitivity.shape[0]
    cycles = sensitivity.shape[1]
    tile = sensitivity.shape[2]
    blocks = pattern.shape[0]
    widths = cycles * tile
    mask_blocks = pattern.astype(jnp.bfloat16)[:, None, :, :]
    masked = (sensitivity.reshape(blocks, tile, cycles, tile) * mask_blocks).reshape(
        rows_here, widths
    )
    weighted = (sample_weight[:, None] * masked.astype(jnp.float32)).astype(jnp.bfloat16)
    first_tile = (
        sensitivity[:, 0, :].reshape(blocks, tile, tile)
        * pattern[:, 0, :].astype(jnp.bfloat16)[:, :, None]
    ).reshape(rows_here, tile)
    row_count = lax.axis_size("row")
    row = lax.axis_index("row")
    col = lax.axis_index("col")
    f32 = jnp.float32

    head_weighted = (sample_weight[:, None] * first_tile.astype(f32)).astype(jnp.bfloat16)
    block = jnp.einsum("sb,sc->bc", first_tile, head_weighted, preferred_element_type=f32)
    prior_row = jnp.where(row == 0, prior, jnp.zeros_like(prior))
    extra = jnp.zeros((8, tile), f32).at[0].set(prior_row)
    own = jnp.concatenate([block, extra], axis=0)
    corner_sum = lax.psum(jnp.where(col == 0, own, jnp.zeros_like(own)), ("row", "col"))
    prior_head = corner_sum[tile]

    tile_src, corner_sum = lax.optimization_barrier((first_tile, corner_sum))
    identity = jnp.eye(tile, dtype=f32)
    corner = corner_sum[:tile] + identity * prior_head[None, :]
    lower = jnp.linalg.cholesky(corner)
    lower_inv = jax.scipy.linalg.solve_triangular(lower, identity, lower=True)
    band = jnp.concatenate(
        [spread(tile_src, "col", owner) for owner in range(row_count)], axis=1
    )
    band, lower_inv = lax.optimization_barrier((band, lower_inv))
    head_tile = band[:, :tile]
    rest = band[:, tile:]
    part_head = jnp.einsum("sb,sc->bc", head_tile, weighted, preferred_element_type=f32)
    rest_weighted = (sample_weight[:, None] * rest.astype(f32)).astype(jnp.bfloat16)
    side = lax.psum(
        jnp.einsum("sb,sc->bc", head_tile, rest_weighted, preferred_element_type=f32), "row"
    ).reshape(tile, row_count - 1, tile)

    hi = lax.Precision.HIGHEST
    corner_inv = jnp.dot(lower_inv.T, lower_inv, precision=hi)
    side_t = jnp.einsum("jri,jk->rik", side, corner_inv, precision=hi)
    transform = jnp.concatenate(
        [lower_inv, -side_t.reshape((row_count - 1) * tile, tile)], axis=0
    )

    part_rest = jnp.einsum("sb,sc->bc", rest, weighted, preferred_element_type=f32)
    chunks = 2 if cycles % 2 == 0 else 1
    span = widths // chunks
    mine = lax.dynamic_slice_in_dim(transform, row * tile, tile, axis=0)
    head_on = (col == 0).astype(f32)
    diag_on = ((col == row) & (row != 0)).astype(f32)
    fix = head_on * mine * prior_head[None, :] + diag_on * identity * prior[None, :]
    pieces = []
    for k in range(chunks):
        cols_k = slice(k * span, (k + 1) * span)
        moved = jnp.dot(transform, part_head[:, cols_k], precision=lax.Precision.HIGH)
        partial = moved + jnp.concatenate(
            [jnp.zeros((tile, span), f32), part_rest[:, cols_k]], axis=0
        )
        piece = lax.psum_scatter(partial, "row", scatter_dimension=0, tiled=True)
        if k == 0:
            piece = piece.at[:, :tile].add(fix)
        pieces.append(piece.reshape(tile, cycles // chunks, tile))
    return jnp.concatenate(pieces, axis=1) if chunks > 1 else pieces[0]


def solution(mesh):
    return jax.shard_map(
        body,
        mesh=mesh,
        in_specs=(P("row", None, "col"), P("row"), P("row", None, "col"), P("row")),
        out_specs=P("row", None, "col"),
        check_vma=False,
    )
```

```python
import jax
import jax.numpy as jnp
from jax import lax
from jax.sharding import PartitionSpec as P


def spread(value, axis, root):
    mine = lax.axis_index(axis) == root
    return lax.psum(jnp.where(mine, value, jnp.zeros_like(value)), axis)


def body(sensitivity, sample_weight, pattern, prior):
    rows_here = sensitivity.shape[0]
    cycles = sensitivity.shape[1]
    tile = sensitivity.shape[2]
    blocks = pattern.shape[0]
    widths = cycles * tile
    mask_blocks = pattern.astype(jnp.bfloat16)[:, None, :, :]
    masked = (sensitivity.reshape(blocks, tile, cycles, tile) * mask_blocks).reshape(
        rows_here, widths
    )
    weighted = (sample_weight[:, None] * masked.astype(jnp.float32)).astype(jnp.bfloat16)
    first_tile = (
        sensitivity[:, 0, :].reshape(blocks, tile, tile)
        * pattern[:, 0, :].astype(jnp.bfloat16)[:, :, None]
    ).reshape(rows_here, tile)
    row_count = lax.axis_size("row")
    row = lax.axis_index("row")
    col = lax.axis_index("col")
    f32 = jnp.float32

    head_tile = spread(first_tile, "col", 0)
    head_weighted = (sample_weight[:, None] * head_tile.astype(f32)).astype(jnp.bfloat16)
    block = jnp.einsum("sb,sc->bc", head_tile, head_weighted, preferred_element_type=f32)
    prior_row = jnp.where(row == 0, prior, jnp.zeros_like(prior))
    extra = jnp.zeros((8, tile), f32).at[0].set(prior_row)
    corner_sum = lax.psum(jnp.concatenate([block, extra], axis=0), "row")
    prior_head = corner_sum[tile]


    part_head = jnp.einsum("sb,sc->bc", head_tile, weighted, preferred_element_type=f32)

    tile_src, corner_sum, part_head = lax.optimization_barrier((first_tile, corner_sum, part_head))
    identity = jnp.eye(tile, dtype=f32)
    corner = corner_sum[:tile] + identity * prior_head[None, :]
    lower = jnp.linalg.cholesky(corner)
    lower_inv = jax.scipy.linalg.solve_triangular(lower, identity, lower=True)
    rest_parts = [spread(tile_src, "col", owner) for owner in range(1, row_count)]
    rest = jnp.concatenate(rest_parts, axis=1)
    rest, lower_inv = lax.optimization_barrier((rest, lower_inv))
    rest_weighted = (sample_weight[:, None] * rest.astype(f32)).astype(jnp.bfloat16)
    side = lax.psum(
        jnp.einsum("sb,sc->bc", head_tile, rest_weighted, preferred_element_type=f32), "row"
    ).reshape(tile, row_count - 1, tile)

    hi = lax.Precision.HIGHEST
    corner_inv = jnp.dot(lower_inv.T, lower_inv, precision=hi)
    side_t = jnp.einsum("jri,jk->rik", side, corner_inv, precision=hi)
    transform = jnp.concatenate(
        [lower_inv, -side_t.reshape((row_count - 1) * tile, tile)], axis=0
    )

    part_rest = jnp.einsum("sb,sc->bc", rest, weighted, preferred_element_type=f32)
    chunks = 1
    span = widths // chunks
    mine = lax.dynamic_slice_in_dim(transform, row * tile, tile, axis=0)
    head_on = (col == 0).astype(f32)
    diag_on = ((col == row) & (row != 0)).astype(f32)
    fix = head_on * mine * prior_head[None, :] + diag_on * identity * prior[None, :]
    pieces = []
    for k in range(chunks):
        cols_k = slice(k * span, (k + 1) * span)
        moved = jnp.dot(transform, part_head[:, cols_k], precision=lax.Precision.HIGH)
        partial = moved + jnp.concatenate(
            [jnp.zeros((tile, span), f32), part_rest[:, cols_k]], axis=0
        )
        piece = lax.psum_scatter(partial, "row", scatter_dimension=0, tiled=True)
        if k == 0:
            piece = piece.at[:, :tile].add(fix)
        pieces.append(piece.reshape(tile, cycles // chunks, tile))
    return jnp.concatenate(pieces, axis=1) if chunks > 1 else pieces[0]


def solution(mesh):
    return jax.shard_map(
        body,
        mesh=mesh,
        in_specs=(P("row", None, "col"), P("row"), P("row", None, "col"), P("row")),
        out_specs=P("row", None, "col"),
        check_vma=False,
    )
```
